32 devices in a mesh: seq: 8 (over y, x, core), tensor: 4 (over z).
Axes of the slice: x: 2, y: 2, z: 4, core: 2. Of those that a mesh axis runs over, the one named last changes fastest.
Arguments:
- queries: bfloat16 [4096, 8192], P('seq', 'tensor')
- image_refs: int32 [4096, 1], P('seq'), may hold values from 0 to 7; in each aligned block of 512 rows (0 to 511, 512 to 1023, ...) at most 128 rows name the same one
- features: bfloat16 [8, 1601, 8192], P('seq', None, 'tensor'), may hold values from -6 to 6
- kv_weight: bfloat16 [8192, 2048], P('tensor'), may hold values from -0.0625 to 0.0625
Outputs:
- attended: bfloat16 [4096, 8192], P('seq', 'tensor')
The draws below stay inside these ranges and needn't reach their ends.
Inputs may be any that keep to these rules, and one draw needn't show every extreme that they name: image_refs holds an image number per text token; at most 128 tokens of one device reference the same image, and some device has an image referenced by exactly 128 of its tokens.
All inputs are finite; a program needn't handle non-finite values.
Results may differ from the reference program's by a relative error of at most 0.03.
Values may be sent and summed in bfloat16 or wider, within the bound.
No kernel may reach another device: no remote copies, remote signals or barrier semaphores. Data moves between devices by JAX's collectives and lax.ppermute only.
A program may use at most 128 MiB of HBM per device.

```python
import math
import jax
import jax.numpy as jnp
import numpy as np
from jax import lax

D = 8192
HEADS = 64
KV_HEADS = 8
HEAD_DIM = 128
IMG_TOK = 1601
TOK_DEV = 512
GROUP = 8
CAP = 128
NIMG = 8
TEXT = 4096
N_SEQ = 8
N_TENSOR = 4


def draw_queries(key, part):
    normal_draw = jax.random.normal(key, (TEXT, HEADS * HEAD_DIM), jnp.float32)
    return normal_draw.astype(jnp.bfloat16)


def level_of(rng, dims, cuts, low, high):
    factor_of = 1.0
    for dim, blocks in cuts:
        heights = jax.random.uniform(jax.random.fold_in(jax.random.fold_in(rng, 6), dim), (blocks,), jnp.float32, low / len(cuts), high / len(cuts))
        factor_of = factor_of * jnp.repeat(jnp.exp(heights), dims[dim] // blocks).reshape((-1,) + (1,) * (len(dims) - 1 - dim))
    return factor_of


def routed_block(own_key, own, number, rows, count, top, reach, lean):
    sequence = jax.random.permutation(own_key, count)
    heavy_load, ordinary = shares(count, rows * top, reach, lean, True), shares(count, rows * top, reach, lean, False)
    places = jnp.arange(count)

    def named(lengths, rotation):
        used = int((lengths > 0).sum())
        fixed = max(1, used // 4)
        passed = fixed + (places - fixed + rotation * (used - fixed)) % max(1, count - fixed)
        return jnp.zeros((count,), jnp.int32).at[sequence[jnp.where(places < fixed, places, passed)]].set(jnp.asarray(lengths, jnp.int32))

    lengths = jnp.where(number % 4 == 0, named(heavy_load, number // 4), named(ordinary, number - number // 4 - 1))
    mixed = jax.random.permutation(jax.random.fold_in(own, 3), count)
    donor, receiver = mixed[0:count // 2 * 2:2], mixed[1:count // 2 * 2:2]
    room = jnp.minimum(lengths[donor] - 1, reach - lengths[receiver]) // 2
    room = jnp.where((donor == sequence[0]) | (receiver == sequence[0]) | (lengths[receiver] == 0), 0, jnp.maximum(room, 0))
    passed = jax.random.randint(jax.random.fold_in(own, 4), (count // 2,), 0, 1 << 20) % (room + 1)
    lengths = lengths.at[donor].add(-passed).at[receiver].add(passed)
    members = jnp.searchsorted(jnp.cumsum(lengths), jnp.arange(rows * top), side="right").astype(jnp.int32)
    grid = members.reshape(top, rows).T
    grid = grid[jax.random.permutation(jax.random.fold_in(own, 1), rows)]
    rotation = jax.random.randint(jax.random.fold_in(own, 2), (rows, 1), 0, top)
    return jnp.take_along_axis(grid, (jnp.arange(top)[None, :] + rotation) % top, axis=1)


def shares(number_of, total, limit, lean, full):
    loads = [(1 << 20) // math.isqrt(standing ** lean) + 1 for standing in range(1, number_of + 1)]
    largest = limit if full else min(limit, max(-(-total // number_of), total * loads[0] // sum(loads)))
    least = 1 if total - largest >= number_of - 1 else 0
    given, surplus = [largest] + [least] * (number_of - 1), total - largest - least * (number_of - 1)
    while surplus > 0:
        movable = [i for i in range(1, number_of) if given[i] < largest] or [i for i in range(1, number_of) if given[i] < limit]
        mass, remaining = sum([loads[i] for i in movable]), surplus
        for i in movable:
            extra = min(limit - given[i], max(1, remaining * loads[i] // mass), surplus)
            given[i] = given[i] + extra
            surplus = surplus - extra
    return np.array(given)


def centred(stream_key, extent, width, bound, cuts=(), kind=jnp.bfloat16):
    values = width * jax.random.normal(stream_key, extent, jnp.float32)
    if cuts:
        values = values * level_of(stream_key, extent, cuts, -0.22, 0.18)
    return jnp.clip(values, -bound, bound).astype(kind)


def setup_inputs(seed: int = 0) -> dict:
    splits = jax.random.split(jax.random.key(seed), 5)
    queries = draw_queries(jax.random.fold_in(splits[4], 71), 0)
    image_refs_keys = jax.random.split(jax.random.fold_in(splits[1], 1), TEXT // TOK_DEV)
    image_refs_turns = jax.random.permutation(jax.random.fold_in(splits[1], 3), TEXT // TOK_DEV)
    image_refs = jax.vmap(lambda own, number: routed_block(jax.random.fold_in(splits[1], 2), own, number, TOK_DEV, NIMG, 1, CAP, 2))(image_refs_keys, image_refs_turns).reshape((TEXT, 1))
    features = centred(splits[2], (NIMG, IMG_TOK, D), 1.0, 6.0, ((0, 8), (2, 4)))
    kv_weight = centred(splits[3], (D, 2 * KV_HEADS * HEAD_DIM), D ** -0.5, 0.0625, ((0, 4),))
    return {"queries": queries, "image_refs": image_refs, "features": features, "kv_weight": kv_weight}


def attend(query_rows, key_values, group, head_dim):
    row_count = query_rows.shape[0]
    query_heads = query_rows.shape[1] // head_dim
    kv_heads = key_values.shape[1] // (2 * head_dim)
    image_len = key_values.shape[0]
    per_head = query_rows.reshape(row_count, query_heads, head_dim).transpose(1, 0, 2)
    split_kv = key_values.reshape(image_len, kv_heads, 2, head_dim)
    key_heads = split_kv[:, :, 0, :].transpose(1, 0, 2)
    value_heads = split_kv[:, :, 1, :].transpose(1, 0, 2)
    score_scale = head_dim ** -0.5

    def one_head(inputs):
        head_query, head_index = inputs
        key_mat = key_heads[head_index // group]
        value_mat = value_heads[head_index // group]
        scores = lax.dot_general(head_query, key_mat, (((1,), (1,)), ((), ())),
                                 preferred_element_type=jnp.float32) * score_scale
        row_max = jnp.max(scores, axis=1, keepdims=True)
        weights_exp = jnp.exp(scores - row_max)
        totals = jnp.sum(weights_exp, axis=1, keepdims=True)
        probs = weights_exp.astype(jnp.bfloat16)
        weighted = jnp.dot(probs, value_mat, preferred_element_type=jnp.float32) / totals
        return weighted.astype(jnp.bfloat16)

    heads_out = lax.map(one_head, (per_head, jnp.arange(query_heads, dtype=jnp.int32)))
    return heads_out.transpose(1, 0, 2).reshape(row_count, query_heads * head_dim)


def project_image(image_block, kv_weight):
    shard_width = D // N_TENSOR
    running_sum = jnp.zeros((image_block.shape[0], kv_weight.shape[1]), jnp.float32)
    for block_num in range(N_TENSOR):
        lower = block_num * shard_width
        partial_term = jnp.dot(image_block[:, lower:lower + shard_width], kv_weight[lower:lower + shard_width],
                               preferred_element_type=jnp.float32).astype(jnp.bfloat16)
        running_sum = running_sum + partial_term.astype(jnp.float32)
    return running_sum.astype(jnp.bfloat16)


def reference(queries, image_refs, features, kv_weight):
    owners = image_refs[:, 0]
    onehot = (owners[:, None] == jnp.arange(NIMG, dtype=jnp.int32)[None, :]).astype(jnp.int32)
    running = jnp.cumsum(onehot.reshape(N_SEQ, TOK_DEV, NIMG), axis=1).reshape(TEXT, NIMG)
    position = jnp.sum(onehot * (running - 1), axis=1).astype(jnp.int32)
    device_of = (jnp.arange(TEXT, dtype=jnp.int32) // TOK_DEV).astype(jnp.int32)
    slot_index = device_of * CAP + position
    slot_table = jnp.full((NIMG, N_SEQ * CAP), TEXT, jnp.int32)
    slot_table = slot_table.at[owners, slot_index].set(jnp.arange(TEXT, dtype=jnp.int32))
    padded_queries = jnp.concatenate([queries, jnp.zeros((1, queries.shape[1]), queries.dtype)], axis=0)

    def per_image(image_num, result):
        key_values = project_image(features[image_num], kv_weight)
        gathered = padded_queries[slot_table[image_num]]
        answered = attend(gathered, key_values, GROUP, HEAD_DIM)
        return result.at[slot_table[image_num]].set(answered)

    result = jnp.zeros((TEXT + 1, queries.shape[1]), jnp.bfloat16)
    result = lax.fori_loop(0, NIMG, per_image, result)
    return result[:TEXT]
```

```python
import functools

import jax
import jax.numpy as jnp
from jax import lax
from jax.experimental import pallas as pl
from jax.experimental.pallas import tpu as pltpu
from jax.sharding import PartitionSpec as P

HEADS = 64
KV_HEADS = 8
HEAD_DIM = 128
ROW_TILE = 256


def attend_kernel(scale, q_ref, k_ref, v_ref, o_ref):
    q = q_ref[...]
    scores = (
        lax.dot_general(
            q, k_ref[...], (((1,), (0,)), ((), ())), preferred_element_type=jnp.float32
        )
        * scale
    )
    row_max = jnp.max(scores, axis=1, keepdims=True)
    weights_exp = jnp.exp(scores - row_max)
    totals = jnp.sum(weights_exp, axis=1, keepdims=True)
    probs = weights_exp.astype(jnp.bfloat16)
    weighted = lax.dot_general(
        probs, v_ref[...], (((1,), (1,)), ((), ())), preferred_element_type=jnp.float32
    )
    o_ref[...] = (weighted / totals).astype(o_ref.dtype)


def attend(query_rows, kv_t, group, head_dim):
    rows, width = query_rows.shape
    query_heads = width // head_dim
    image_len = kv_t.shape[1]
    tile = min(ROW_TILE, rows)
    assert rows % tile == 0
    scale = head_dim ** (-0.5)
    flops = 4 * rows * query_heads * image_len * head_dim
    return pl.pallas_call(
        functools.partial(attend_kernel, scale),
        out_shape=jax.ShapeDtypeStruct((rows, width), jnp.bfloat16),
        grid=(query_heads, rows // tile),
        in_specs=[
            pl.BlockSpec((tile, head_dim), lambda h, i: (i, h)),
            pl.BlockSpec((head_dim, image_len), lambda h, i: (2 * (h // group), 0)),
            pl.BlockSpec((head_dim, image_len), lambda h, i: (2 * (h // group) + 1, 0)),
        ],
        out_specs=pl.BlockSpec((tile, head_dim), lambda h, i: (i, h)),
        compiler_params=pltpu.CompilerParams(
            dimension_semantics=("arbitrary", "arbitrary"),
            vmem_limit_bytes=48 * 1024 * 1024,
        ),
        cost_estimate=pl.CostEstimate(
            flops=flops,
            transcendentals=rows * query_heads * image_len,
            bytes_accessed=2 * (2 * rows * width + kv_t.size),
        ),
    )(query_rows, kv_t, kv_t)


def on_device(queries, image_refs, features, kv_weight):
    seq_devices = lax.axis_size("seq")
    token_count = queries.shape[0]
    width_cols = queries.shape[1]
    capacity = 2 * token_count // seq_devices
    owners = image_refs[:, 0]
    onehot = (owners[:, None] == jnp.arange(seq_devices, dtype=jnp.int32)[None, :]).astype(
        jnp.int32
    )
    running = jnp.cumsum(onehot, axis=0)
    position = jnp.sum(onehot * (running - 1), axis=1)
    slot_index = owners * capacity + position
    outgoing = (
        jnp.zeros((seq_devices * capacity, width_cols), jnp.bfloat16).at[slot_index].set(queries)
    )
    outgoing = outgoing.reshape(seq_devices, capacity, width_cols)
    group = HEADS // KV_HEADS
    image_block = features[0]
    kv_t = lax.psum_scatter(
        lax.dot_general(
            kv_weight, image_block, (((0,), (1,)), ((), ())), preferred_element_type=jnp.float32
        ).astype(jnp.bfloat16),
        "tensor",
        scatter_dimension=0,
        tiled=True,
    )
    received = lax.all_to_all(outgoing, "seq", split_axis=0, concat_axis=0, tiled=True)
    flat_rows = received.reshape(-1, width_cols)
    answered = attend(flat_rows, kv_t, group, HEAD_DIM).reshape(received.shape)
    returned = lax.all_to_all(answered, "seq", split_axis=0, concat_axis=0, tiled=True)
    return returned.reshape(seq_devices * capacity, width_cols)[slot_index]


def solution(mesh):
    placed = (P("seq", "tensor"), P("seq", None), P("seq", None, "tensor"), P("tensor", None))
    return jax.shard_map(
        on_device, mesh=mesh, in_specs=placed, out_specs=P("seq", "tensor"), check_vma=False
    )
```

```python
import functools

import jax
import jax.numpy as jnp
from jax import lax
from jax.experimental import pallas as pl
from jax.experimental.pallas import tpu as pltpu
from jax.sharding import PartitionSpec as P

HEADS = 64
KV_HEADS = 8
HEAD_DIM = 128
ROW_TILE = 256


def attend_kernel(scale, q_ref, k_ref, v_ref, o_ref):
    q = q_ref[...]
    scores = (
        lax.dot_general(
            q, k_ref[...], (((1,), (1,)), ((), ())), preferred_element_type=jnp.float32
        )
        * scale
    )
    row_max = jnp.max(scores, axis=1, keepdims=True)
    weights_exp = jnp.exp(scores - row_max)
    totals = jnp.sum(weights_exp, axis=1, keepdims=True)
    probs = weights_exp.astype(jnp.bfloat16)
    weighted = jnp.dot(probs, v_ref[...], preferred_element_type=jnp.float32)
    o_ref[...] = (weighted / totals).astype(o_ref.dtype)


def attend(query_rows, key_values, group, head_dim, first_head):
    rows = query_rows.shape[0]
    query_heads = group
    width = group * head_dim
    image_len = key_values.shape[0]
    tile = min(ROW_TILE, rows)
    assert rows % tile == 0
    scale = head_dim ** (-0.5)
    flops = 4 * rows * query_heads * image_len * head_dim
    return pl.pallas_call(
        functools.partial(attend_kernel, scale),
        out_shape=jax.ShapeDtypeStruct((rows, width), jnp.bfloat16),
        grid=(query_heads, rows // tile),
        in_specs=[
            pl.BlockSpec((tile, head_dim), lambda h, i: (i, first_head + h)),
            pl.BlockSpec((image_len, head_dim), lambda h, i: (0, 0)),
            pl.BlockSpec((image_len, head_dim), lambda h, i: (0, 1)),
        ],
        out_specs=pl.BlockSpec((tile, head_dim), lambda h, i: (i, h)),
        compiler_params=pltpu.CompilerParams(
            dimension_semantics=("arbitrary", "arbitrary"),
            vmem_limit_bytes=48 * 1024 * 1024,
        ),
        cost_estimate=pl.CostEstimate(
            flops=flops,
            transcendentals=rows * query_heads * image_len,
            bytes_accessed=2 * (2 * rows * width + key_values.size),
        ),
    )(query_rows, key_values, key_values)


def on_device(queries, image_refs, features, kv_weight):
    seq_devices = lax.axis_size("seq")
    token_count = queries.shape[0]
    width_cols = queries.shape[1]
    capacity = 2 * token_count // seq_devices
    owners = image_refs[:, 0]
    onehot = (owners[:, None] == jnp.arange(seq_devices, dtype=jnp.int32)[None, :]).astype(
        jnp.int32
    )
    running = jnp.cumsum(onehot, axis=0)
    position = jnp.sum(onehot * (running - 1), axis=1)
    slot_index = owners * capacity + position
    outgoing = (
        jnp.zeros((seq_devices * capacity, width_cols), jnp.bfloat16).at[slot_index].set(queries)
    )
    outgoing = outgoing.reshape(seq_devices, capacity, width_cols)
    group = HEADS // KV_HEADS
    image_block = features[0]
    tensor_devices = lax.axis_size("tensor")
    local_kv = KV_HEADS // tensor_devices
    split_weight = kv_weight.reshape(kv_weight.shape[0], tensor_devices, local_kv, 2 * HEAD_DIM)
    received = lax.all_to_all(outgoing, "seq", split_axis=0, concat_axis=0, tiled=True)
    flat_rows = received.reshape(-1, width_cols)
    pieces = []
    for head in range(local_kv):
        weight_part = split_weight[:, :, head, :].reshape(kv_weight.shape[0], -1)
        key_values = lax.psum_scatter(
            jnp.dot(image_block, weight_part, preferred_element_type=jnp.float32).astype(
                jnp.bfloat16
            ),
            "tensor",
            scatter_dimension=1,
            tiled=True,
        )
        answered = attend(flat_rows, key_values, group, HEAD_DIM, head * group)
        answered = answered.reshape(seq_devices, capacity, -1)
        returned = lax.all_to_all(answered, "seq", split_axis=0, concat_axis=0, tiled=True)
        pieces.append(returned.reshape(seq_devices * capacity, -1)[slot_index])
    return jnp.concatenate(pieces, axis=1)


def solution(mesh):
    placed = (P("seq", "tensor"), P("seq", None), P("seq", None, "tensor"), P("tensor", None))
    return jax.shard_map(
        on_device, mesh=mesh, in_specs=placed, out_specs=P("seq", "tensor"), check_vma=False
    )
```

```python
import functools

import jax
import jax.numpy as jnp
from jax import lax
from jax.experimental import pallas as pl
from jax.experimental.pallas import tpu as pltpu
from jax.sharding import PartitionSpec as P

HEADS = 64
KV_HEADS = 8
HEAD_DIM = 128
ROW_TILE = 256


def attend_kernel(scale, q_ref, k_ref, v_ref, o_ref):
    head_dim = o_ref.shape[1]
    q = q_ref[...]
    scores = (
        lax.dot_general(
            q, k_ref[...], (((1,), (1,)), ((), ())), preferred_element_type=jnp.float32
        )
        * scale
    )
    row_max = jnp.max(scores, axis=1, keepdims=True)
    weights_exp = jnp.exp(scores - row_max)
    probs = weights_exp.astype(jnp.bfloat16)
    weighted = jnp.dot(probs, v_ref[...], preferred_element_type=jnp.float32)
    totals = weighted[:, head_dim : head_dim + 1]
    o_ref[...] = (weighted[:, :head_dim] / totals).astype(o_ref.dtype)


def attend(query_rows, key_values, group, head_dim, first_head):
    rows = query_rows.shape[0]
    query_heads = group
    width = group * head_dim
    image_len = key_values.shape[0]
    values_ones = jnp.concatenate(
        [key_values[:, head_dim:], jnp.ones((image_len, head_dim), key_values.dtype)], axis=1
    )
    tile = min(ROW_TILE, rows)
    assert rows % tile == 0
    scale = head_dim ** (-0.5)
    flops = 6 * rows * query_heads * image_len * head_dim
    return pl.pallas_call(
        functools.partial(attend_kernel, scale),
        out_shape=jax.ShapeDtypeStruct((rows, width), jnp.bfloat16),
        grid=(query_heads, rows // tile),
        in_specs=[
            pl.BlockSpec((tile, head_dim), lambda h, i: (i, first_head + h)),
            pl.BlockSpec((image_len, head_dim), lambda h, i: (0, 0)),
            pl.BlockSpec((image_len, 2 * head_dim), lambda h, i: (0, 0)),
        ],
        out_specs=pl.BlockSpec((tile, head_dim), lambda h, i: (i, h)),
        compiler_params=pltpu.CompilerParams(
            dimension_semantics=("arbitrary", "arbitrary"),
            vmem_limit_bytes=48 * 1024 * 1024,
        ),
        cost_estimate=pl.CostEstimate(
            flops=flops,
            transcendentals=rows * query_heads * image_len,
            bytes_accessed=2 * (2 * rows * width + key_values.size),
        ),
    )(query_rows, key_values, values_ones)


def on_device(queries, image_refs, features, kv_weight):
    seq_devices = lax.axis_size("seq")
    token_count = queries.shape[0]
    width_cols = queries.shape[1]
    capacity = 2 * token_count // seq_devices
    owners = image_refs[:, 0]
    onehot = (owners[:, None] == jnp.arange(seq_devices, dtype=jnp.int32)[None, :]).astype(
        jnp.int32
    )
    running = jnp.cumsum(onehot, axis=0)
    position = jnp.sum(onehot * (running - 1), axis=1)
    slot_index = owners * capacity + position
    outgoing = (
        jnp.zeros((seq_devices * capacity, width_cols), jnp.bfloat16).at[slot_index].set(queries)
    )
    outgoing = outgoing.reshape(seq_devices, capacity, width_cols)
    group = HEADS // KV_HEADS
    image_block = features[0]
    tensor_devices = lax.axis_size("tensor")
    local_kv = KV_HEADS // tensor_devices
    projected = jnp.dot(image_block, kv_weight, preferred_element_type=jnp.float32).astype(
        jnp.bfloat16
    )
    kv_width = 2 * HEAD_DIM
    received = lax.all_to_all(outgoing, "seq", split_axis=0, concat_axis=0, tiled=True)
    flat_rows = received.reshape(-1, width_cols)
    pieces = []
    for head in range(local_kv):
        key_values = lax.psum_scatter(
            jnp.concatenate(
                [
                    projected[:, (dest * local_kv + head) * kv_width :][:, :kv_width]
                    for dest in range(tensor_devices)
                ],
                axis=1,
            ),
            "tensor",
            scatter_dimension=1,
            tiled=True,
        )
        answered = attend(flat_rows, key_values, group, HEAD_DIM, head * group)
        answered = answered.reshape(seq_devices, capacity, -1)
        returned = lax.all_to_all(answered, "seq", split_axis=0, concat_axis=0, tiled=True)
        pieces.append(returned.reshape(seq_devices * capacity, -1)[slot_index])
    return jnp.concatenate(pieces, axis=1)


def solution(mesh):
    placed = (P("seq", "tensor"), P("seq", None), P("seq", None, "tensor"), P("tensor", None))
    return jax.shard_map(
        on_device, mesh=mesh, in_specs=placed, out_specs=P("seq", "tensor"), check_vma=False
    )
```

```python
import functools

import jax
import jax.numpy as jnp
from jax import lax
from jax.experimental import pallas as pl
from jax.experimental.pallas import tpu as pltpu
from jax.sharding import PartitionSpec as P

HEADS = 64
KV_HEADS = 8
HEAD_DIM = 128
ROW_TILE = 256


def attend_kernel(scale, tiles_ref, q_ref, k_ref, v_ref, o_ref):
    @pl.when(pl.program_id(1) < tiles_ref[0])
    def _():
        q = q_ref[...]
        scores = (
            lax.dot_general(
                q, k_ref[...], (((1,), (1,)), ((), ())), preferred_element_type=jnp.float32
            )
            * scale
        )
        row_max = jnp.max(scores, axis=1, keepdims=True)
        weights_exp = jnp.exp(scores - row_max)
        totals = jnp.sum(weights_exp, axis=1, keepdims=True)
        probs = weights_exp.astype(jnp.bfloat16)
        weighted = jnp.dot(probs, v_ref[...], preferred_element_type=jnp.float32)
        o_ref[...] = (weighted / totals).astype(o_ref.dtype)


def attend(query_rows, key_values, group, head_dim, first_head, live_tiles, tile):
    rows = query_rows.shape[0]
    query_heads = group
    width = group * head_dim
    image_len = key_values.shape[0]
    assert rows % tile == 0
    scale = head_dim ** (-0.5)
    flops = 4 * rows * query_heads * image_len * head_dim

    def row_block(i, tiles):
        return jnp.minimum(i, tiles[0] - 1)

    return pl.pallas_call(
        functools.partial(attend_kernel, scale),
        out_shape=jax.ShapeDtypeStruct((rows, width), jnp.bfloat16),
        grid_spec=pltpu.PrefetchScalarGridSpec(
            num_scalar_prefetch=1,
            grid=(query_heads, rows // tile),
            in_specs=[
                pl.BlockSpec((tile, head_dim), lambda h, i, t: (row_block(i, t), first_head + h)),
                pl.BlockSpec((image_len, head_dim), lambda h, i, t: (0, 0)),
                pl.BlockSpec((image_len, head_dim), lambda h, i, t: (0, 1)),
            ],
            out_specs=pl.BlockSpec((tile, head_dim), lambda h, i, t: (row_block(i, t), h)),
        ),
        compiler_params=pltpu.CompilerParams(
            dimension_semantics=("arbitrary", "arbitrary"),
            vmem_limit_bytes=48 * 1024 * 1024,
        ),
        cost_estimate=pl.CostEstimate(
            flops=flops // 2,
            transcendentals=rows * query_heads * image_len // 2,
            bytes_accessed=2 * (rows * width + key_values.size),
        ),
    )(live_tiles, query_rows, key_values, key_values)


def on_device(queries, image_refs, features, kv_weight):
    seq_devices = lax.axis_size("seq")
    token_count = queries.shape[0]
    width_cols = queries.shape[1]
    capacity = 2 * token_count // seq_devices
    rows = seq_devices * capacity
    tile = min(ROW_TILE, rows)
    owners = image_refs[:, 0]
    onehot = (owners[:, None] == jnp.arange(seq_devices, dtype=jnp.int32)[None, :]).astype(
        jnp.int32
    )
    running = jnp.cumsum(onehot, axis=0)
    position = jnp.sum(onehot * (running - 1), axis=1)
    slot_index = owners * capacity + position
    outgoing = (
        jnp.zeros((rows, width_cols), jnp.bfloat16).at[slot_index].set(queries)
    )
    outgoing = outgoing.reshape(seq_devices, capacity, width_cols)
    sent_counts = jnp.sum(onehot, axis=0).reshape(seq_devices, 1)
    counts = lax.all_to_all(sent_counts, "seq", split_axis=0, concat_axis=0, tiled=True)[:, 0]
    ends = jnp.cumsum(counts)
    starts = ends - counts
    total = ends[-1]
    live_tiles = jnp.maximum((total + tile - 1) // tile, 1).astype(jnp.int32).reshape(1)
    packed = jnp.arange(rows, dtype=jnp.int32)
    source = jnp.minimum(
        jnp.sum((ends[None, :] <= packed[:, None]).astype(jnp.int32), axis=1), seq_devices - 1
    )
    packed_slot = jnp.where(packed < total, source * capacity + packed - starts[source], 0)
    slot_source = packed // capacity
    slot_offset = packed % capacity
    slot_packed = jnp.where(
        slot_offset < counts[slot_source], starts[slot_source] + slot_offset, 0
    )

    group = HEADS // KV_HEADS
    image_block = features[0]
    tensor_devices = lax.axis_size("tensor")
    local_kv = KV_HEADS // tensor_devices
    projected = jnp.dot(image_block, kv_weight, preferred_element_type=jnp.float32).astype(
        jnp.bfloat16
    )
    kv_width = 2 * HEAD_DIM
    received = lax.all_to_all(outgoing, "seq", split_axis=0, concat_axis=0, tiled=True)
    packed_rows = received.reshape(-1, width_cols)[packed_slot]
    pieces = []
    for head in range(local_kv):
        key_values = lax.psum_scatter(
            jnp.concatenate(
                [
                    projected[:, (dest * local_kv + head) * kv_width :][:, :kv_width]
                    for dest in range(tensor_devices)
                ],
                axis=1,
            ),
            "tensor",
            scatter_dimension=1,
            tiled=True,
        )
        answered = attend(packed_rows, key_values, group, HEAD_DIM, head * group, live_tiles, tile)
        answered = answered[slot_packed].reshape(seq_devices, capacity, -1)
        returned = lax.all_to_all(answered, "seq", split_axis=0, concat_axis=0, tiled=True)
        pieces.append(returned.reshape(rows, -1)[slot_index])
    return jnp.concatenate(pieces, axis=1)


def solution(mesh):
    placed = (P("seq", "tensor"), P("seq", None), P("seq", None, "tensor"), P("tensor", None))
    return jax.shard_map(
        on_device, mesh=mesh, in_specs=placed, out_specs=P("seq", "tensor"), check_vma=False
    )
```

```python
import functools

import jax
import jax.numpy as jnp
from jax import lax
from jax.experimental import pallas as pl
from jax.experimental.pallas import tpu as pltpu
from jax.sharding import PartitionSpec as P

HEADS = 64
KV_HEADS = 8
HEAD_DIM = 128
ROW_TILE = 256


def attend_kernel(scale, group, head_dim, tiles_ref, q_ref, k_ref, v_ref, o_ref):
    @pl.when(pl.program_id(0) < tiles_ref[0])
    def _():
        keys = k_ref[...]
        values = v_ref[...]
        for head in range(group):
            columns = slice(head * head_dim, (head + 1) * head_dim)
            scores = (
                lax.dot_general(
                    q_ref[:, columns],
                    keys,
                    (((1,), (1,)), ((), ())),
                    preferred_element_type=jnp.float32,
                )
                * scale
            )
            row_max = jnp.max(scores, axis=1, keepdims=True)
            weights_exp = jnp.exp(scores - row_max)
            totals = jnp.sum(weights_exp, axis=1, keepdims=True)
            probs = weights_exp.astype(jnp.bfloat16)
            weighted = jnp.dot(probs, values, preferred_element_type=jnp.float32)
            o_ref[:, columns] = (weighted / totals).astype(o_ref.dtype)


def attend(query_rows, key_values, group, head_dim, first_head, live_tiles, tile):
    rows = query_rows.shape[0]
    width = group * head_dim
    image_len = key_values.shape[0]
    assert rows % tile == 0 and first_head % group == 0
    scale = head_dim ** (-0.5)
    flops = 4 * rows * group * image_len * head_dim

    def row_block(i, tiles):
        return jnp.minimum(i, tiles[0] - 1)

    return pl.pallas_call(
        functools.partial(attend_kernel, scale, group, head_dim),
        out_shape=jax.ShapeDtypeStruct((rows, width), jnp.bfloat16),
        grid_spec=pltpu.PrefetchScalarGridSpec(
            num_scalar_prefetch=1,
            grid=(rows // tile,),
            in_specs=[
                pl.BlockSpec((tile, width), lambda i, t: (row_block(i, t), first_head // group)),
                pl.BlockSpec((image_len, head_dim), lambda i, t: (0, 0)),
                pl.BlockSpec((image_len, head_dim), lambda i, t: (0, 1)),
            ],
            out_specs=pl.BlockSpec((tile, width), lambda i, t: (row_block(i, t), 0)),
        ),
        compiler_params=pltpu.CompilerParams(
            dimension_semantics=("arbitrary",),
            vmem_limit_bytes=48 * 1024 * 1024,
        ),
        cost_estimate=pl.CostEstimate(
            flops=flops // 2,
            transcendentals=rows * group * image_len // 2,
            bytes_accessed=2 * (rows * width + key_values.size),
        ),
    )(live_tiles, query_rows, key_values, key_values)


def on_device(queries, image_refs, features, kv_weight):
    seq_devices = lax.axis_size("seq")
    token_count = queries.shape[0]
    width_cols = queries.shape[1]
    capacity = 2 * token_count // seq_devices
    rows = seq_devices * capacity
    tile = min(ROW_TILE, rows)
    owners = image_refs[:, 0]
    onehot = (owners[:, None] == jnp.arange(seq_devices, dtype=jnp.int32)[None, :]).astype(
        jnp.int32
    )
    running = jnp.cumsum(onehot, axis=0)
    position = jnp.sum(onehot * (running - 1), axis=1)
    slot_index = owners * capacity + position
    outgoing = (
        jnp.zeros((rows, width_cols), jnp.bfloat16).at[slot_index].set(queries)
    )
    outgoing = outgoing.reshape(seq_devices, capacity, width_cols)
    sent_counts = jnp.sum(onehot, axis=0).reshape(seq_devices, 1)
    counts = lax.all_to_all(sent_counts, "seq", split_axis=0, concat_axis=0, tiled=True)[:, 0]
    ends = jnp.cumsum(counts)
    starts = ends - counts
    total = ends[-1]
    live_tiles = jnp.maximum((total + tile - 1) // tile, 1).astype(jnp.int32).reshape(1)
    packed = jnp.arange(rows, dtype=jnp.int32)
    source = jnp.minimum(
        jnp.sum((ends[None, :] <= packed[:, None]).astype(jnp.int32), axis=1), seq_devices - 1
    )
    packed_slot = jnp.where(packed < total, source * capacity + packed - starts[source], 0)
    slot_source = packed // capacity
    slot_offset = packed % capacity
    slot_packed = jnp.where(
        slot_offset < counts[slot_source], starts[slot_source] + slot_offset, 0
    )

    group = HEADS // KV_HEADS
    image_block = features[0]
    tensor_devices = lax.axis_size("tensor")
    local_kv = KV_HEADS // tensor_devices
    projected = jnp.dot(image_block, kv_weight, preferred_element_type=jnp.float32).astype(
        jnp.bfloat16
    )
    kv_width = 2 * HEAD_DIM
    received = lax.all_to_all(outgoing, "seq", split_axis=0, concat_axis=0, tiled=True)
    packed_rows = received.reshape(-1, width_cols)[packed_slot]
    pieces = []
    for head in range(local_kv):
        key_values = lax.psum_scatter(
            jnp.concatenate(
                [
                    projected[:, (dest * local_kv + head) * kv_width :][:, :kv_width]
                    for dest in range(tensor_devices)
                ],
                axis=1,
            ),
            "tensor",
            scatter_dimension=1,
            tiled=True,
        )
        answered = attend(packed_rows, key_values, group, HEAD_DIM, head * group, live_tiles, tile)
        answered = answered[slot_packed].reshape(seq_devices, capacity, -1)
        returned = lax.all_to_all(answered, "seq", split_axis=0, concat_axis=0, tiled=True)
        pieces.append(returned.reshape(rows, -1)[slot_index])
    return jnp.concatenate(pieces, axis=1)


def solution(mesh):
    placed = (P("seq", "tensor"), P("seq", None), P("seq", None, "tensor"), P("tensor", None))
    return jax.shard_map(
        on_device, mesh=mesh, in_specs=placed, out_specs=P("seq", "tensor"), check_vma=False
    )
```

```python
import functools

import jax
import jax.numpy as jnp
from jax import lax
from jax.experimental import pallas as pl
from jax.experimental.pallas import tpu as pltpu
from jax.sharding import PartitionSpec as P

HEADS = 64
KV_HEADS = 8
HEAD_DIM = 128
ROW_TILE = 256


def attend_kernel(scale, group, head_dim, tiles_ref, q_ref, k_ref, v_ref, o_ref):
    @pl.when(pl.program_id(0) < tiles_ref[0])
    def _():
        keys = k_ref[...]
        values = v_ref[...]

        def one_head(head, carry):
            columns = pl.ds(pl.multiple_of(head * head_dim, head_dim), head_dim)
            scores = (
                lax.dot_general(
                    q_ref[:, columns],
                    keys,
                    (((1,), (1,)), ((), ())),
                    preferred_element_type=jnp.float32,
                )
                * scale
            )
            row_max = jnp.max(scores, axis=1, keepdims=True)
            weights_exp = jnp.exp(scores - row_max)
            totals = jnp.sum(weights_exp, axis=1, keepdims=True)
            probs = weights_exp.astype(jnp.bfloat16)
            weighted = jnp.dot(probs, values, preferred_element_type=jnp.float32)
            o_ref[:, columns] = (weighted / totals).astype(o_ref.dtype)
            return carry

        lax.fori_loop(0, group, one_head, 0)


def attend(query_rows, key_values, group, head_dim, first_head, live_tiles, tile, pad_rows):
    rows = query_rows.shape[0] - pad_rows
    width = group * head_dim
    image_len = key_values.shape[0]
    assert rows % tile == 0 and first_head % group == 0
    scale = head_dim ** (-0.5)
    flops = 4 * rows * group * image_len * head_dim

    def row_block(i, tiles):
        return jnp.minimum(i, tiles[0] - 1)

    return pl.pallas_call(
        functools.partial(attend_kernel, scale, group, head_dim),
        out_shape=jax.ShapeDtypeStruct((rows + pad_rows, width), jnp.bfloat16),
        grid_spec=pltpu.PrefetchScalarGridSpec(
            num_scalar_prefetch=1,
            grid=(rows // tile,),
            in_specs=[
                pl.BlockSpec((tile, width), lambda i, t: (row_block(i, t), first_head // group)),
                pl.BlockSpec((image_len, head_dim), lambda i, t: (0, 0)),
                pl.BlockSpec((image_len, head_dim), lambda i, t: (0, 1)),
            ],
            out_specs=pl.BlockSpec((tile, width), lambda i, t: (row_block(i, t), 0)),
        ),
        compiler_params=pltpu.CompilerParams(
            dimension_semantics=("arbitrary",),
            vmem_limit_bytes=48 * 1024 * 1024,
        ),
        cost_estimate=pl.CostEstimate(
            flops=flops // 2,
            transcendentals=rows * group * image_len // 2,
            bytes_accessed=2 * (rows * width + key_values.size),
        ),
    )(live_tiles, query_rows, key_values, key_values)


def on_device(queries, image_refs, features, kv_weight):
    seq_devices = lax.axis_size("seq")
    token_count = queries.shape[0]
    width_cols = queries.shape[1]
    capacity = 2 * token_count // seq_devices
    rows = seq_devices * capacity
    tile = min(ROW_TILE, rows)
    owners = image_refs[:, 0]
    onehot = (owners[:, None] == jnp.arange(seq_devices, dtype=jnp.int32)[None, :]).astype(
        jnp.int32
    )
    running = jnp.cumsum(onehot, axis=0)
    position = jnp.sum(onehot * (running - 1), axis=1)
    slot_index = owners * capacity + position
    outgoing = (
        jnp.zeros((rows, width_cols), jnp.bfloat16).at[slot_index].set(queries)
    )
    outgoing = outgoing.reshape(seq_devices, capacity, width_cols)
    sent_counts = jnp.sum(onehot, axis=0).reshape(seq_devices, 1)
    counts = lax.all_to_all(sent_counts, "seq", split_axis=0, concat_axis=0, tiled=True)[:, 0]
    ends = jnp.cumsum(counts)
    starts = ends - counts
    total = ends[-1]
    live_tiles = jnp.maximum((total + tile - 1) // tile, 1).astype(jnp.int32).reshape(1)
    group = HEADS // KV_HEADS
    image_block = features[0]
    tensor_devices = lax.axis_size("tensor")
    local_kv = KV_HEADS // tensor_devices
    projected = jnp.dot(image_block, kv_weight, preferred_element_type=jnp.float32).astype(
        jnp.bfloat16
    )
    kv_width = 2 * HEAD_DIM
    received = lax.all_to_all(outgoing, "seq", split_axis=0, concat_axis=0, tiled=True)
    packed_rows = jnp.zeros((rows + capacity, width_cols), jnp.bfloat16)
    for src in range(seq_devices):
        packed_rows = lax.dynamic_update_slice(packed_rows, received[src], (starts[src], 0))
    pieces = []
    for head in range(local_kv):
        key_values = lax.psum_scatter(
            jnp.concatenate(
                [
                    projected[:, (dest * local_kv + head) * kv_width :][:, :kv_width]
                    for dest in range(tensor_devices)
                ],
                axis=1,
            ),
            "tensor",
            scatter_dimension=1,
            tiled=True,
        )
        answered = attend(
            packed_rows, key_values, group, HEAD_DIM, head * group, live_tiles, tile, capacity
        )
        answered = jnp.stack(
            [
                lax.dynamic_slice_in_dim(answered, starts[src], capacity, axis=0)
                for src in range(seq_devices)
            ]
        )
        returned = lax.all_to_all(answered, "seq", split_axis=0, concat_axis=0, tiled=True)
        pieces.append(returned.reshape(rows, -1)[slot_index])
    return jnp.concatenate(pieces, axis=1)


def solution(mesh):
    placed = (P("seq", "tensor"), P("seq", None), P("seq", None, "tensor"), P("tensor", None))
    return jax.shard_map(
        on_device, mesh=mesh, in_specs=placed, out_specs=P("seq", "tensor"), check_vma=False
    )
```

```python
import functools

import jax
import jax.numpy as jnp
from jax import lax
from jax.experimental import pallas as pl
from jax.experimental.pallas import tpu as pltpu
from jax.sharding import PartitionSpec as P

HEADS = 64
KV_HEADS = 8
HEAD_DIM = 128
ROW_TILE = 256


def attend_kernel(scale, group, head_dim, tiles_ref, q_ref, k_ref, v_ref, o_ref):
    @pl.when(pl.program_id(0) < tiles_ref[0])
    def _():
        keys = k_ref[...]
        values = v_ref[...]

        def one_head(head, carry):
            columns = pl.ds(pl.multiple_of(head * head_dim, head_dim), head_dim)
            scores = (
                lax.dot_general(
                    q_ref[:, columns],
                    keys,
                    (((1,), (1,)), ((), ())),
                    preferred_element_type=jnp.float32,
                )
                * scale
            )
            row_max = jnp.max(scores, axis=1, keepdims=True)
            weights_exp = jnp.exp(scores - row_max)
            totals = jnp.sum(weights_exp, axis=1, keepdims=True)
            probs = weights_exp.astype(jnp.bfloat16)
            weighted = jnp.dot(probs, values, preferred_element_type=jnp.float32)
            o_ref[:, columns] = (weighted / totals).astype(o_ref.dtype)
            return carry

        lax.fori_loop(0, group, one_head, 0)


def attend(query_rows, key_values, group, head_dim, first_head, live_tiles, tile):
    rows = query_rows.shape[0]
    width = group * head_dim
    image_len = key_values.shape[0]
    assert rows % tile == 0 and first_head % group == 0
    scale = head_dim ** (-0.5)
    flops = 4 * rows * group * image_len * head_dim

    def row_block(i, tiles):
        return jnp.minimum(i, tiles[0] - 1)

    return pl.pallas_call(
        functools.partial(attend_kernel, scale, group, head_dim),
        out_shape=jax.ShapeDtypeStruct((rows, width), jnp.bfloat16),
        grid_spec=pltpu.PrefetchScalarGridSpec(
            num_scalar_prefetch=1,
            grid=(rows // tile,),
            in_specs=[
                pl.BlockSpec((tile, width), lambda i, t: (row_block(i, t), first_head // group)),
                pl.BlockSpec((image_len, head_dim), lambda i, t: (0, 0)),
                pl.BlockSpec((image_len, head_dim), lambda i, t: (0, 1)),
            ],
            out_specs=pl.BlockSpec((tile, width), lambda i, t: (row_block(i, t), 0)),
        ),
        compiler_params=pltpu.CompilerParams(
            dimension_semantics=("arbitrary",),
            vmem_limit_bytes=48 * 1024 * 1024,
        ),
        cost_estimate=pl.CostEstimate(
            flops=flops // 2,
            transcendentals=rows * group * image_len // 2,
            bytes_accessed=2 * (rows * width + key_values.size),
        ),
    )(live_tiles, query_rows, key_values, key_values)


def on_device(queries, image_refs, features, kv_weight):
    seq_devices = lax.axis_size("seq")
    token_count = queries.shape[0]
    width_cols = queries.shape[1]
    capacity = 2 * token_count // seq_devices
    rows = seq_devices * capacity
    tile = min(ROW_TILE, rows)
    owners = image_refs[:, 0]
    onehot = (owners[:, None] == jnp.arange(seq_devices, dtype=jnp.int32)[None, :]).astype(
        jnp.int32
    )
    running = jnp.cumsum(onehot, axis=0)
    position = jnp.sum(onehot * (running - 1), axis=1)
    slot_index = owners * capacity + position
    outgoing = (
        jnp.zeros((rows, width_cols), jnp.bfloat16).at[slot_index].set(queries)
    )
    outgoing = outgoing.reshape(seq_devices, capacity, width_cols)
    sent_counts = jnp.sum(onehot, axis=0).reshape(seq_devices, 1)
    counts = lax.all_to_all(sent_counts, "seq", split_axis=0, concat_axis=0, tiled=True)[:, 0]
    ends = jnp.cumsum(counts)
    starts = ends - counts
    total = ends[-1]
    live_tiles = jnp.maximum((total + tile - 1) // tile, 1).astype(jnp.int32).reshape(1)
    packed = jnp.arange(rows, dtype=jnp.int32)
    source = jnp.minimum(
        jnp.sum((ends[None, :] <= packed[:, None]).astype(jnp.int32), axis=1), seq_devices - 1
    )
    packed_slot = jnp.where(packed < total, source * capacity + packed - starts[source], 0)
    slot_source = packed // capacity
    slot_offset = packed % capacity
    slot_packed = jnp.where(
        slot_offset < counts[slot_source], starts[slot_source] + slot_offset, 0
    )

    group = HEADS // KV_HEADS
    image_block = features[0]
    tensor_devices = lax.axis_size("tensor")
    local_kv = KV_HEADS // tensor_devices
    kv_width = 2 * HEAD_DIM
    head_split = 2
    call_heads = group // head_split
    received = lax.all_to_all(outgoing, "seq", split_axis=0, concat_axis=0, tiled=True)
    packed_rows = received.reshape(-1, width_cols)[packed_slot]
    pieces = []
    for head in range(local_kv):
        weight_part = jnp.concatenate(
            [
                kv_weight[:, (dest * local_kv + head) * kv_width :][:, :kv_width]
                for dest in range(tensor_devices)
            ],
            axis=1,
        )
        key_values = lax.psum_scatter(
            jnp.dot(image_block, weight_part, preferred_element_type=jnp.float32).astype(
                jnp.bfloat16
            ),
            "tensor",
            scatter_dimension=1,
            tiled=True,
        )
        for part in range(head_split):
            first = head * group + part * call_heads
            answered = attend(packed_rows, key_values, call_heads, HEAD_DIM, first, live_tiles, tile)
            answered = answered[slot_packed].reshape(seq_devices, capacity, -1)
            returned = lax.all_to_all(answered, "seq", split_axis=0, concat_axis=0, tiled=True)
            pieces.append(returned.reshape(rows, -1)[slot_index])
    return jnp.concatenate(pieces, axis=1)


def solution(mesh):
    placed = (P("seq", "tensor"), P("seq", None), P("seq", None, "tensor"), P("tensor", None))
    return jax.shard_map(
        on_device, mesh=mesh, in_specs=placed, out_specs=P("seq", "tensor"), check_vma=False
    )
```

```python
import functools

import jax
import jax.numpy as jnp
from jax import lax
from jax.experimental import pallas as pl
from jax.experimental.pallas import tpu as pltpu
from jax.sharding import PartitionSpec as P

HEADS = 64
KV_HEADS = 8
HEAD_DIM = 128
ROW_TILE = 256


def attend_kernel(scale, group, head_dim, tiles_ref, q_ref, k_ref, v_ref, o_ref):
    @pl.when(pl.program_id(0) < tiles_ref[0])
    def _():
        keys = k_ref[...]
        values = v_ref[...]

        def one_head(head, carry):
            columns = pl.ds(pl.multiple_of(head * head_dim, head_dim), head_dim)
            scores = (
                lax.dot_general(
                    q_ref[:, columns],
                    keys,
                    (((1,), (1,)), ((), ())),
                    preferred_element_type=jnp.float32,
                )
                * scale
            )
            row_max = jnp.max(scores, axis=1, keepdims=True)
            weights_exp = jnp.exp(scores - row_max)
            totals = jnp.sum(weights_exp, axis=1, keepdims=True)
            probs = weights_exp.astype(jnp.bfloat16)
            weighted = jnp.dot(probs, values, preferred_element_type=jnp.float32)
            o_ref[:, columns] = (weighted / totals).astype(o_ref.dtype)
            return carry

        lax.fori_loop(0, group, one_head, 0)


def attend(query_rows, key_values, group, head_dim, first_head, live_tiles, tile):
    rows = query_rows.shape[0]
    width = group * head_dim
    image_len = key_values.shape[0]
    assert rows % tile == 0 and first_head % group == 0
    scale = head_dim ** (-0.5)
    flops = 4 * rows * group * image_len * head_dim

    def row_block(i, tiles):
        return jnp.minimum(i, tiles[0] - 1)

    return pl.pallas_call(
        functools.partial(attend_kernel, scale, group, head_dim),
        out_shape=jax.ShapeDtypeStruct((rows, width), jnp.bfloat16),
        grid_spec=pltpu.PrefetchScalarGridSpec(
            num_scalar_prefetch=1,
            grid=(rows // tile,),
            in_specs=[
                pl.BlockSpec((tile, width), lambda i, t: (row_block(i, t), first_head // group)),
                pl.BlockSpec((image_len, head_dim), lambda i, t: (0, 0)),
                pl.BlockSpec((image_len, head_dim), lambda i, t: (0, 1)),
            ],
            out_specs=pl.BlockSpec((tile, width), lambda i, t: (row_block(i, t), 0)),
        ),
        compiler_params=pltpu.CompilerParams(
            dimension_semantics=("arbitrary",),
            vmem_limit_bytes=48 * 1024 * 1024,
        ),
        cost_estimate=pl.CostEstimate(
            flops=flops // 2,
            transcendentals=rows * group * image_len // 2,
            bytes_accessed=2 * (rows * width + key_values.size),
        ),
    )(live_tiles, query_rows, key_values, key_values)


def on_device(queries, image_refs, features, kv_weight):
    seq_devices = lax.axis_size("seq")
    token_count = queries.shape[0]
    width_cols = queries.shape[1]
    capacity = 2 * token_count // seq_devices
    rows = seq_devices * capacity
    tile = min(ROW_TILE, rows)
    owners = image_refs[:, 0]
    onehot = (owners[:, None] == jnp.arange(seq_devices, dtype=jnp.int32)[None, :]).astype(
        jnp.int32
    )
    running = jnp.cumsum(onehot, axis=0)
    position = jnp.sum(onehot * (running - 1), axis=1)
    slot_index = owners * capacity + position
    outgoing = (
        jnp.zeros((rows, width_cols), jnp.bfloat16).at[slot_index].set(queries)
    )
    outgoing = outgoing.reshape(seq_devices, capacity, width_cols)
    sent_counts = jnp.sum(onehot, axis=0).reshape(seq_devices, 1)
    counts = lax.all_to_all(sent_counts, "seq", split_axis=0, concat_axis=0, tiled=True)[:, 0]
    ends = jnp.cumsum(counts)
    starts = ends - counts
    total = ends[-1]
    live_tiles = jnp.maximum((total + tile - 1) // tile, 1).astype(jnp.int32).reshape(1)
    packed = jnp.arange(rows, dtype=jnp.int32)
    source = jnp.minimum(
        jnp.sum((ends[None, :] <= packed[:, None]).astype(jnp.int32), axis=1), seq_devices - 1
    )
    packed_slot = jnp.where(packed < total, source * capacity + packed - starts[source], 0)
    slot_source = packed // capacity
    slot_offset = packed % capacity
    slot_packed = jnp.where(
        slot_offset < counts[slot_source], starts[slot_source] + slot_offset, 0
    )

    group = HEADS // KV_HEADS
    image_block = features[0]
    tensor_devices = lax.axis_size("tensor")
    local_kv = KV_HEADS // tensor_devices
    kv_width = 2 * HEAD_DIM
    received = lax.all_to_all(outgoing, "seq", split_axis=0, concat_axis=0, tiled=True)
    packed_rows = received.reshape(-1, width_cols)[packed_slot]
    pieces = []
    for head in range(local_kv):
        weight_part = jnp.concatenate(
            [
                kv_weight[:, (dest * local_kv + head) * kv_width :][:, :kv_width]
                for dest in range(tensor_devices)
            ],
            axis=1,
        )
        key_values = lax.psum_scatter(
            jnp.dot(image_block, weight_part, preferred_element_type=jnp.float32).astype(
                jnp.bfloat16
            ),
            "tensor",
            scatter_dimension=1,
            tiled=True,
        )
        answered = attend(packed_rows, key_values, group, HEAD_DIM, head * group, live_tiles, tile)
        answered = answered[slot_packed].reshape(seq_devices, capacity, -1)
        returned = lax.all_to_all(answered, "seq", split_axis=0, concat_axis=0, tiled=True)
        pieces.append(returned.reshape(rows, -1)[slot_index])
    return jnp.concatenate(pieces, axis=1)


def solution(mesh):
    placed = (P("seq", "tensor"), P("seq", None), P("seq", None, "tensor"), P("tensor", None))
    return jax.shard_map(
        on_device, mesh=mesh, in_specs=placed, out_specs=P("seq", "tensor"), check_vma=False
    )
```

```python
import functools

import jax
import jax.numpy as jnp
from jax import lax
from jax.experimental import pallas as pl
from jax.experimental.pallas import tpu as pltpu
from jax.sharding import PartitionSpec as P

HEADS = 64
KV_HEADS = 8
HEAD_DIM = 128
ROW_TILE = 256


def attend_kernel(group, head_dim, tiles_ref, q_ref, k_ref, v_ref, o_ref):
    @pl.when(pl.program_id(0) < tiles_ref[0])
    def _():
        keys = k_ref[...]
        values = v_ref[...]
        for head in range(group):
            columns = slice(head * head_dim, (head + 1) * head_dim)
            scores = lax.dot_general(
                q_ref[:, columns], keys, (((1,), (1,)), ((), ())), preferred_element_type=jnp.float32
            )
            row_max = jnp.max(scores, axis=1, keepdims=True)
            weights_exp = jnp.exp(scores - row_max)
            totals = jnp.sum(weights_exp, axis=1, keepdims=True)
            probs = weights_exp.astype(jnp.bfloat16)
            weighted = jnp.dot(probs, values, preferred_element_type=jnp.float32)
            o_ref[:, columns] = (weighted / totals).astype(o_ref.dtype)


def attend(query_rows, key_values, group, head_dim, first_head, live_tiles, tile):
    rows = query_rows.shape[0]
    width = group * head_dim
    image_len = key_values.shape[0]
    assert rows % tile == 0 and first_head % group == 0
    flops = 4 * rows * group * image_len * head_dim

    def row_block(i, tiles):
        return jnp.minimum(i, tiles[0] - 1)

    return pl.pallas_call(
        functools.partial(attend_kernel, group, head_dim),
        out_shape=jax.ShapeDtypeStruct((rows, width), jnp.bfloat16),
        grid_spec=pltpu.PrefetchScalarGridSpec(
            num_scalar_prefetch=1,
            grid=(rows // tile,),
            in_specs=[
                pl.BlockSpec((tile, width), lambda i, t: (row_block(i, t), first_head // group)),
                pl.BlockSpec((image_len, head_dim), lambda i, t: (0, 0)),
                pl.BlockSpec((image_len, head_dim), lambda i, t: (0, 1)),
            ],
            out_specs=pl.BlockSpec((tile, width), lambda i, t: (row_block(i, t), 0)),
        ),
        compiler_params=pltpu.CompilerParams(
            dimension_semantics=("arbitrary",),
            vmem_limit_bytes=48 * 1024 * 1024,
        ),
        cost_estimate=pl.CostEstimate(
            flops=flops // 2,
            transcendentals=rows * group * image_len // 2,
            bytes_accessed=2 * (rows * width + key_values.size),
        ),
    )(live_tiles, query_rows, key_values, key_values)


def on_device(queries, image_refs, features, kv_weight):
    seq_devices = lax.axis_size("seq")
    token_count = queries.shape[0]
    width_cols = queries.shape[1]
    capacity = 2 * token_count // seq_devices
    rows = seq_devices * capacity
    tile = min(ROW_TILE, rows)
    owners = image_refs[:, 0]
    onehot = (owners[:, None] == jnp.arange(seq_devices, dtype=jnp.int32)[None, :]).astype(
        jnp.int32
    )
    running = jnp.cumsum(onehot, axis=0)
    position = jnp.sum(onehot * (running - 1), axis=1)
    slot_index = owners * capacity + position
    outgoing = (
        jnp.zeros((rows, width_cols), jnp.bfloat16).at[slot_index].set(queries)
    )
    outgoing = outgoing.reshape(seq_devices, capacity, width_cols)
    sent_counts = jnp.sum(onehot, axis=0).reshape(seq_devices, 1)
    counts = lax.all_to_all(sent_counts, "seq", split_axis=0, concat_axis=0, tiled=True)[:, 0]
    ends = jnp.cumsum(counts)
    starts = ends - counts
    total = ends[-1]
    live_tiles = jnp.maximum((total + tile - 1) // tile, 1).astype(jnp.int32).reshape(1)
    packed = jnp.arange(rows, dtype=jnp.int32)
    source = jnp.minimum(
        jnp.sum((ends[None, :] <= packed[:, None]).astype(jnp.int32), axis=1), seq_devices - 1
    )
    packed_slot = jnp.where(packed < total, source * capacity + packed - starts[source], 0)
    slot_source = packed // capacity
    slot_offset = packed % capacity
    slot_packed = jnp.where(
        slot_offset < counts[slot_source], starts[slot_source] + slot_offset, 0
    )

    group = HEADS // KV_HEADS
    image_block = features[0]
    tensor_devices = lax.axis_size("tensor")
    local_kv = KV_HEADS // tensor_devices
    projected = jnp.dot(image_block, kv_weight, preferred_element_type=jnp.float32).astype(
        jnp.bfloat16
    )
    kv_width = 2 * HEAD_DIM
    received = lax.all_to_all(outgoing, "seq", split_axis=0, concat_axis=0, tiled=True)
    score_scale = HEAD_DIM ** (-0.5)
    packed_rows = (
        received.reshape(-1, width_cols)[packed_slot].astype(jnp.float32) * score_scale
    ).astype(jnp.bfloat16)
    pieces = []
    for head in range(local_kv):
        key_values = lax.psum_scatter(
            jnp.concatenate(
                [
                    projected[:, (dest * local_kv + head) * kv_width :][:, :kv_width]
                    for dest in range(tensor_devices)
                ],
                axis=1,
            ),
            "tensor",
            scatter_dimension=1,
            tiled=True,
        )
        answered = attend(packed_rows, key_values, group, HEAD_DIM, head * group, live_tiles, tile)
        answered = answered[slot_packed].reshape(seq_devices, capacity, -1)
        returned = lax.all_to_all(answered, "seq", split_axis=0, concat_axis=0, tiled=True)
        pieces.append(returned.reshape(rows, -1)[slot_index])
    return jnp.concatenate(pieces, axis=1)


def solution(mesh):
    placed = (P("seq", "tensor"), P("seq", None), P("seq", None, "tensor"), P("tensor", None))
    return jax.shard_map(
        on_device, mesh=mesh, in_specs=placed, out_specs=P("seq", "tensor"), check_vma=False
    )
```

```python
import functools

import jax
import jax.numpy as jnp
from jax import lax
from jax.experimental import pallas as pl
from jax.experimental.pallas import tpu as pltpu
from jax.sharding import PartitionSpec as P

HEADS = 64
KV_HEADS = 8
HEAD_DIM = 128
ROW_TILE = 256


def attend_kernel(group, head_dim, q_ref, k_ref, v_ref, o_ref):
    if True:
        keys = k_ref[...]
        values = v_ref[...]
        for head in range(group):
            columns = slice(head * head_dim, (head + 1) * head_dim)
            scores = lax.dot_general(
                q_ref[:, columns], keys, (((1,), (1,)), ((), ())), preferred_element_type=jnp.float32
            )
            row_max = jnp.max(scores, axis=1, keepdims=True)
            weights_exp = jnp.exp(scores - row_max)
            totals = jnp.sum(weights_exp, axis=1, keepdims=True)
            probs = weights_exp.astype(jnp.bfloat16)
            weighted = jnp.dot(probs, values, preferred_element_type=jnp.float32)
            o_ref[:, columns] = (weighted / totals).astype(o_ref.dtype)


def attend(query_rows, key_values, group, head_dim, first_head, tile):
    rows = query_rows.shape[0]
    width = group * head_dim
    image_len = key_values.shape[0]
    assert rows % tile == 0 and first_head % group == 0
    flops = 4 * rows * group * image_len * head_dim
    return pl.pallas_call(
        functools.partial(attend_kernel, group, head_dim),
        out_shape=jax.ShapeDtypeStruct((rows, width), jnp.bfloat16),
        grid=(rows // tile,),
        in_specs=[
            pl.BlockSpec((tile, width), lambda i: (i, first_head // group)),
            pl.BlockSpec((image_len, head_dim), lambda i: (0, 0)),
            pl.BlockSpec((image_len, head_dim), lambda i: (0, 1)),
        ],
        out_specs=pl.BlockSpec((tile, width), lambda i: (i, 0)),
        compiler_params=pltpu.CompilerParams(
            dimension_semantics=("arbitrary",),
            vmem_limit_bytes=48 * 1024 * 1024,
        ),
        cost_estimate=pl.CostEstimate(
            flops=flops,
            transcendentals=rows * group * image_len,
            bytes_accessed=2 * (2 * rows * width + key_values.size),
        ),
    )(query_rows, key_values, key_values)


def on_device(queries, image_refs, features, kv_weight):
    seq_devices = lax.axis_size("seq")
    token_count = queries.shape[0]
    width_cols = queries.shape[1]
    capacity = 2 * token_count // seq_devices
    rows = seq_devices * capacity
    tile = min(ROW_TILE, rows)
    owners = image_refs[:, 0]
    onehot = (owners[:, None] == jnp.arange(seq_devices, dtype=jnp.int32)[None, :]).astype(
        jnp.int32
    )
    running = jnp.cumsum(onehot, axis=0)
    position = jnp.sum(onehot * (running - 1), axis=1)
    slot_index = owners * capacity + position
    outgoing = (
        jnp.zeros((rows, width_cols), jnp.bfloat16).at[slot_index].set(queries)
    )
    outgoing = outgoing.reshape(seq_devices, capacity, width_cols)
    group = HEADS // KV_HEADS
    image_block = features[0]
    tensor_devices = lax.axis_size("tensor")
    local_kv = KV_HEADS // tensor_devices
    projected = jnp.dot(image_block, kv_weight, preferred_element_type=jnp.float32).astype(
        jnp.bfloat16
    )
    kv_width = 2 * HEAD_DIM
    received = lax.all_to_all(outgoing, "seq", split_axis=0, concat_axis=0, tiled=True)
    score_scale = HEAD_DIM ** (-0.5)
    scaled_rows = (received.reshape(-1, width_cols).astype(jnp.float32) * score_scale).astype(
        jnp.bfloat16
    )
    result = None
    for head in range(local_kv):
        key_values = lax.psum_scatter(
            jnp.concatenate(
                [
                    projected[:, (dest * local_kv + head) * kv_width :][:, :kv_width]
                    for dest in range(tensor_devices)
                ],
                axis=1,
            ),
            "tensor",
            scatter_dimension=1,
            tiled=True,
        )
        answered = attend(scaled_rows, key_values, group, HEAD_DIM, head * group, tile)
        answered = answered.reshape(seq_devices, capacity, -1)
        returned = lax.all_to_all(answered, "seq", split_axis=0, concat_axis=0, tiled=True)
        piece = returned.reshape(rows, -1)[slot_index]
        if result is None:
            result = jnp.zeros((token_count, width_cols), jnp.bfloat16)
        result = lax.dynamic_update_slice(result, piece, (0, head * piece.shape[1]))
    return result


def solution(mesh):
    placed = (P("seq", "tensor"), P("seq", None), P("seq", None, "tensor"), P("tensor", None))
    return jax.shard_map(
        on_device, mesh=mesh, in_specs=placed, out_specs=P("seq", "tensor"), check_vma=False
    )
```

```python
import functools

import jax
import jax.numpy as jnp
from jax import lax
from jax.experimental import pallas as pl
from jax.experimental.pallas import tpu as pltpu
from jax.sharding import PartitionSpec as P

HEADS = 64
KV_HEADS = 8
HEAD_DIM = 128
ROW_TILE = 256


def attend_kernel(group, head_dim, q_ref, k_ref, v_ref, o_ref):
    if True:
        keys = k_ref[...]
        values = v_ref[...]
        for head in range(group):
            columns = slice(head * head_dim, (head + 1) * head_dim)
            scores = lax.dot_general(
                q_ref[:, columns], keys, (((1,), (1,)), ((), ())), preferred_element_type=jnp.float32
            )
            row_max = jnp.max(scores, axis=1, keepdims=True)
            weights_exp = jnp.exp(scores - row_max)
            totals = jnp.sum(weights_exp, axis=1, keepdims=True)
            probs = weights_exp.astype(jnp.bfloat16)
            weighted = jnp.dot(probs, values, preferred_element_type=jnp.float32)
            o_ref[:, columns] = (weighted / totals).astype(o_ref.dtype)


def attend(query_rows, key_values, group, head_dim, first_head, tile):
    rows = query_rows.shape[0]
    width = group * head_dim
    image_len = key_values.shape[0]
    assert rows % tile == 0 and first_head % group == 0
    flops = 4 * rows * group * image_len * head_dim
    return pl.pallas_call(
        functools.partial(attend_kernel, group, head_dim),
        out_shape=jax.ShapeDtypeStruct((rows, width), jnp.bfloat16),
        grid=(rows // tile,),
        in_specs=[
            pl.BlockSpec((tile, width), lambda i: (i, first_head // group)),
            pl.BlockSpec((image_len, head_dim), lambda i: (0, 0)),
            pl.BlockSpec((image_len, head_dim), lambda i: (0, 1)),
        ],
        out_specs=pl.BlockSpec((tile, width), lambda i: (i, 0)),
        compiler_params=pltpu.CompilerParams(
            dimension_semantics=("arbitrary",),
            vmem_limit_bytes=48 * 1024 * 1024,
        ),
        cost_estimate=pl.CostEstimate(
            flops=flops,
            transcendentals=rows * group * image_len,
            bytes_accessed=2 * (2 * rows * width + key_values.size),
        ),
    )(query_rows, key_values, key_values)


def on_device(queries, image_refs, features, kv_weight):
    seq_devices = lax.axis_size("seq")
    token_count = queries.shape[0]
    width_cols = queries.shape[1]
    capacity = 2 * token_count // seq_devices
    rows = seq_devices * capacity
    tile = min(ROW_TILE, rows)
    owners = image_refs[:, 0]
    onehot = (owners[:, None] == jnp.arange(seq_devices, dtype=jnp.int32)[None, :]).astype(
        jnp.int32
    )
    running = jnp.cumsum(onehot, axis=0)
    position = jnp.sum(onehot * (running - 1), axis=1)
    slot_index = owners * capacity + position
    outgoing = (
        jnp.zeros((rows, width_cols), jnp.bfloat16).at[slot_index].set(queries)
    )
    outgoing = outgoing.reshape(seq_devices, capacity, width_cols)
    group = HEADS // KV_HEADS
    image_block = features[0]
    tensor_devices = lax.axis_size("tensor")
    local_kv = KV_HEADS // tensor_devices
    kv_width = 2 * HEAD_DIM
    received = lax.all_to_all(outgoing, "seq", split_axis=0, concat_axis=0, tiled=True)
    score_scale = HEAD_DIM ** (-0.5)
    scaled_rows = (received.reshape(-1, width_cols).astype(jnp.float32) * score_scale).astype(
        jnp.bfloat16
    )
    result = None
    for head in range(local_kv):
        weight_part = jnp.concatenate(
            [
                kv_weight[:, (dest * local_kv + head) * kv_width :][:, :kv_width]
                for dest in range(tensor_devices)
            ],
            axis=1,
        )
        key_values = lax.psum_scatter(
            jnp.dot(image_block, weight_part, preferred_element_type=jnp.float32).astype(
                jnp.bfloat16
            ),
            "tensor",
            scatter_dimension=1,
            tiled=True,
        )
        answered = attend(scaled_rows, key_values, group, HEAD_DIM, head * group, tile)
        answered = answered.reshape(seq_devices, capacity, -1)
        returned = lax.all_to_all(answered, "seq", split_axis=0, concat_axis=0, tiled=True)
        piece = returned.reshape(rows, -1)[slot_index]
        if result is None:
            result = jnp.zeros((token_count, width_cols), jnp.bfloat16)
        result = lax.dynamic_update_slice(result, piece, (0, head * piece.shape[1]))
    return result


def solution(mesh):
    placed = (P("seq", "tensor"), P("seq", None), P("seq", None, "tensor"), P("tensor", None))
    return jax.shard_map(
        on_device, mesh=mesh, in_specs=placed, out_specs=P("seq", "tensor"), check_vma=False
    )
```

```python
import functools

import jax
import jax.numpy as jnp
from jax import lax
from jax.experimental import pallas as pl
from jax.experimental.pallas import tpu as pltpu
from jax.sharding import PartitionSpec as P

HEADS = 64
KV_HEADS = 8
HEAD_DIM = 128
ROW_TILE = 256


def attend_kernel(group, head_dim, q_ref, k_ref, v_ref, o_ref):
    if True:
        keys = k_ref[...]
        values = v_ref[...]
        for head in range(group):
            columns = slice(head * head_dim, (head + 1) * head_dim)
            scores = lax.dot_general(
                q_ref[:, columns], keys, (((1,), (1,)), ((), ())), preferred_element_type=jnp.float32
            )
            row_max = jnp.max(scores, axis=1, keepdims=True)
            weights_exp = jnp.exp(scores - row_max)
            totals = jnp.sum(weights_exp, axis=1, keepdims=True)
            probs = weights_exp.astype(jnp.bfloat16)
            weighted = jnp.dot(probs, values, preferred_element_type=jnp.float32)
            o_ref[:, columns] = (weighted / totals).astype(o_ref.dtype)


def attend(query_rows, key_values, group, head_dim, first_head, tile):
    rows = query_rows.shape[0]
    width = group * head_dim
    image_len = key_values.shape[0]
    assert rows % tile == 0 and first_head % group == 0
    flops = 4 * rows * group * image_len * head_dim
    return pl.pallas_call(
        functools.partial(attend_kernel, group, head_dim),
        out_shape=jax.ShapeDtypeStruct((rows, width), jnp.bfloat16),
        grid=(rows // tile,),
        in_specs=[
            pl.BlockSpec((tile, width), lambda i: (i, first_head // group)),
            pl.BlockSpec((image_len, head_dim), lambda i: (0, 0)),
            pl.BlockSpec((image_len, head_dim), lambda i: (0, 1)),
        ],
        out_specs=pl.BlockSpec((tile, width), lambda i: (i, 0)),
        compiler_params=pltpu.CompilerParams(
            dimension_semantics=("arbitrary",),
            vmem_limit_bytes=48 * 1024 * 1024,
        ),
        cost_estimate=pl.CostEstimate(
            flops=flops,
            transcendentals=rows * group * image_len,
            bytes_accessed=2 * (2 * rows * width + key_values.size),
        ),
    )(query_rows, key_values, key_values)


def on_device(queries, image_refs, features, kv_weight):
    seq_devices = lax.axis_size("seq")
    token_count = queries.shape[0]
    width_cols = queries.shape[1]
    capacity = 2 * token_count // seq_devices
    rows = seq_devices * capacity
    tile = min(ROW_TILE, rows)
    owners = image_refs[:, 0]
    onehot = (owners[:, None] == jnp.arange(seq_devices, dtype=jnp.int32)[None, :]).astype(
        jnp.int32
    )
    running = jnp.cumsum(onehot, axis=0)
    position = jnp.sum(onehot * (running - 1), axis=1)
    slot_index = owners * capacity + position
    outgoing = (
        jnp.zeros((rows, width_cols), jnp.bfloat16).at[slot_index].set(queries)
    )
    outgoing = outgoing.reshape(seq_devices, capacity, width_cols)
    group = HEADS // KV_HEADS
    image_block = features[0]
    tensor_devices = lax.axis_size("tensor")
    local_kv = KV_HEADS // tensor_devices
    kv_width = 2 * HEAD_DIM
    received = lax.all_to_all(outgoing, "seq", split_axis=0, concat_axis=0, tiled=True)
    score_scale = HEAD_DIM ** (-0.5)
    scaled_rows = (received.reshape(-1, width_cols).astype(jnp.float32) * score_scale).astype(
        jnp.bfloat16
    )
    result = None
    for head in range(local_kv):
        weight_part = jnp.concatenate(
            [
                kv_weight[:, (dest * local_kv + head) * kv_width :][:, :kv_width]
                for dest in range(tensor_devices)
            ],
            axis=1,
        )
        key_values = lax.psum_scatter(
            jnp.dot(image_block, weight_part, preferred_element_type=jnp.float32).astype(
                jnp.bfloat16
            ),
            "tensor",
            scatter_dimension=1,
            tiled=True,
        )
        calls = 2
        call_heads = group // calls
        for part in range(calls):
            first = head * group + part * call_heads
            answered = attend(scaled_rows, key_values, call_heads, HEAD_DIM, first, tile)
            answered = answered.reshape(seq_devices, capacity, -1)
            returned = lax.all_to_all(answered, "seq", split_axis=0, concat_axis=0, tiled=True)
            piece = returned.reshape(rows, -1)[slot_index]
            if result is None:
                result = jnp.zeros((token_count, width_cols), jnp.bfloat16)
            result = lax.dynamic_update_slice(result, piece, (0, first * HEAD_DIM))
    return result


def solution(mesh):
    placed = (P("seq", "tensor"), P("seq", None), P("seq", None, "tensor"), P("tensor", None))
    return jax.shard_map(
        on_device, mesh=mesh, in_specs=placed, out_specs=P("seq", "tensor"), check_vma=False
    )
```

```python
import functools

import jax
import jax.numpy as jnp
from jax import lax
from jax.experimental import pallas as pl
from jax.experimental.pallas import tpu as pltpu
from jax.sharding import PartitionSpec as P

HEADS = 64
KV_HEADS = 8
HEAD_DIM = 128
ROW_TILE = 256


def attend_kernel(group, head_dim, q_ref, k_ref, v_ref, o_ref):
    if True:
        keys = k_ref[...]
        values = v_ref[...]
        for head in range(group):
            columns = slice(head * head_dim, (head + 1) * head_dim)
            scores = lax.dot_general(
                q_ref[:, columns], keys, (((1,), (1,)), ((), ())), preferred_element_type=jnp.float32
            )
            row_max = jnp.max(scores, axis=1, keepdims=True)
            weights_exp = jnp.exp(scores - row_max)
            totals = jnp.sum(weights_exp, axis=1, keepdims=True)
            probs = weights_exp.astype(jnp.bfloat16)
            weighted = jnp.dot(probs, values, preferred_element_type=jnp.float32)
            o_ref[:, columns] = (weighted / totals).astype(o_ref.dtype)


def attend(query_rows, key_values, group, head_dim, first_head, tile):
    rows = query_rows.shape[0]
    width = group * head_dim
    image_len = key_values.shape[0]
    assert rows % tile == 0 and first_head % group == 0
    flops = 4 * rows * group * image_len * head_dim
    return pl.pallas_call(
        functools.partial(attend_kernel, group, head_dim),
        out_shape=jax.ShapeDtypeStruct((rows, width), jnp.bfloat16),
        grid=(rows // tile,),
        in_specs=[
            pl.BlockSpec((tile, width), lambda i: (i, first_head // group)),
            pl.BlockSpec((image_len, head_dim), lambda i: (0, 0)),
            pl.BlockSpec((image_len, head_dim), lambda i: (0, 1)),
        ],
        out_specs=pl.BlockSpec((tile, width), lambda i: (i, 0)),
        compiler_params=pltpu.CompilerParams(
            dimension_semantics=("arbitrary",),
            vmem_limit_bytes=67043328,
        ),
        cost_estimate=pl.CostEstimate(
            flops=flops,
            transcendentals=rows * group * image_len,
            bytes_accessed=2 * (2 * rows * width + key_values.size),
        ),
    )(query_rows, key_values, key_values)


def on_device(queries, image_refs, features, kv_weight):
    seq_devices = lax.axis_size("seq")
    token_count = queries.shape[0]
    width_cols = queries.shape[1]
    capacity = 2 * token_count // seq_devices
    rows = seq_devices * capacity
    tile = min(ROW_TILE, rows)
    owners = image_refs[:, 0]
    onehot = (owners[:, None] == jnp.arange(seq_devices, dtype=jnp.int32)[None, :]).astype(
        jnp.int32
    )
    running = jnp.cumsum(onehot, axis=0)
    position = jnp.sum(onehot * (running - 1), axis=1)
    slot_index = owners * capacity + position
    outgoing = (
        jnp.zeros((rows, width_cols), jnp.bfloat16).at[slot_index].set(queries)
    )
    outgoing = outgoing.reshape(seq_devices, capacity, width_cols)
    group = HEADS // KV_HEADS
    image_block = features[0]
    tensor_devices = lax.axis_size("tensor")
    local_kv = KV_HEADS // tensor_devices
    kv_width = 2 * HEAD_DIM
    received = lax.all_to_all(outgoing, "seq", split_axis=0, concat_axis=0, tiled=True)
    score_scale = HEAD_DIM ** (-0.5)
    scaled_rows = (received.reshape(-1, width_cols).astype(jnp.float32) * score_scale).astype(
        jnp.bfloat16
    )
    result = None
    for head in range(local_kv):
        weight_part = jnp.concatenate(
            [
                kv_weight[:, (dest * local_kv + head) * kv_width :][:, :kv_width]
                for dest in range(tensor_devices)
            ],
            axis=1,
        )
        key_values = lax.psum_scatter(
            jnp.dot(image_block, weight_part, preferred_element_type=jnp.float32).astype(
                jnp.bfloat16
            ),
            "tensor",
            scatter_dimension=1,
            tiled=True,
        )
        calls = 2
        call_heads = group // calls
        for part in range(calls):
            first = head * group + part * call_heads
            answered = attend(scaled_rows, key_values, call_heads, HEAD_DIM, first, tile)
            answered = answered.reshape(seq_devices, capacity, -1)
            returned = lax.all_to_all(answered, "seq", split_axis=0, concat_axis=0, tiled=True)
            piece = returned.reshape(rows, -1)[slot_index]
            if result is None:
                result = jnp.zeros((token_count, width_cols), jnp.bfloat16)
            result = lax.dynamic_update_slice(result, piece, (0, first * HEAD_DIM))
    return result


def solution(mesh):
    placed = (P("seq", "tensor"), P("seq", None), P("seq", None, "tensor"), P("tensor", None))
    return jax.shard_map(
        on_device, mesh=mesh, in_specs=placed, out_specs=P("seq", "tensor"), check_vma=False
    )
```
